256 devices in a mesh: rad: 16 (over x, y_hi, core), azi: 16 (over z, y_lo).
Axes of the slice: x: 4, y: 4 (y_hi: 2, y_lo: 2; y = y_hi * 2 + y_lo), z: 8, core: 2. Of those that a mesh axis runs over, the one named last changes fastest.
Arguments:
- fields: float32 [5, 512, 256, 128], P(None, 'rad', 'azi'), may hold values from -6 to 6
- kappa: float32 [512, 256, 128], P('rad', 'azi'), may hold values from 0.01 to 0.1
- radial_speed: float32 [5, 512], P(None, 'rad'), may hold values from -0.5 to 0.5
- azimuth_speed: float32 [5, 512], P(None, 'rad'), may hold values from -0.5 to 0.5
- shifts: int32 [512], P('rad'), may hold values from 0 to 255
Outputs:
- advanced: float32 [5, 512, 256, 128], P(None, 'rad', 'azi')
The draws below stay inside these ranges and needn't reach their ends.
All inputs are finite; a program needn't handle non-finite values.
Results may differ from the reference program's by a relative error of at most 0.00002.
Values sent between devices are 32-bit elements; how exact they have to be, the bound alone decides.
No kernel may reach another device: no remote copies, remote signals or barrier semaphores. Data moves between devices by JAX's collectives and lax.ppermute only.
A program may use at most 64 MiB of HBM per device.

```python
import math
import jax
import jax.numpy as jnp
from jax import lax

F = 5
NZ = 128
NR = 512
NA = 256


def with_ends(values, key, low, top_value):
    longest = values.shape.index(max(values.shape))
    spots = []
    for shift in (0, 1):
        where = [jax.random.randint(jax.random.fold_in(key, axis), (), 0, length) for axis, length in enumerate(values.shape)]
        where[longest] = (where[longest] + shift) % values.shape[longest]
        spots.append(tuple(where))
    return values.at[spots[0]].set(low).at[spots[1]].set(top_value)


def level_of(own_key, extent, pieces, low, high):
    factor_of, own = 1.0, jax.random.fold_in(own_key, 6)
    for position, parts in pieces:
        steps = jnp.exp(jax.random.uniform(jax.random.fold_in(own, position), (parts,), jnp.float32, low / len(pieces), high / len(pieces)))
        factor_of = factor_of * jnp.repeat(steps, extent[position] // parts).reshape([-1 if axis == position else 1 for axis in range(len(extent))])
    return factor_of


def normal_values(rng, extent, scale, limit, cuts=(), kind=jnp.bfloat16):
    factor_of = level_of(rng, extent, cuts, -0.22, 0.18) if cuts else 1.0
    result = jax.random.normal(rng, extent, jnp.float32) * scale * factor_of
    return jnp.minimum(jnp.maximum(result, -limit), limit).astype(kind)


def setup_inputs(seed: int = 0) -> dict:
    key_list = jax.random.split(jax.random.key(seed), 6)
    fields = normal_values(key_list[0], (F, NR, NA, NZ), 1.0, 6.0, ((1, 16), (2, 16)), jnp.float32)
    kappa = jnp.clip(jnp.exp(math.log(0.1) - 2.3025851 * jax.random.uniform(key_list[1], (NR, NA, NZ), jnp.float32) ** level_of(key_list[1], (NR, NA, NZ), ((0, 16), (1, 16)), -0.2, 0.2)), 0.01, 0.1)
    radial_speed = jnp.clip(jax.random.uniform(key_list[2], (F, NR), jnp.float32, -0.5, 0.5) * level_of(key_list[2], (F, NR), ((1, 16),), -0.4, 0.0), -0.5, 0.5)
    azimuth_speed = jnp.clip(jax.random.uniform(key_list[3], (F, NR), jnp.float32, -0.5, 0.5) * level_of(key_list[3], (F, NR), ((1, 16),), -0.4, 0.0), -0.5, 0.5)
    shifts = with_ends(jax.random.randint(key_list[4], (NR,), 0, NA), jax.random.fold_in(key_list[4], 1), 0, NA - 1).astype(jnp.int32)
    return dict(fields=fields, kappa=kappa, radial_speed=radial_speed, azimuth_speed=azimuth_speed, shifts=shifts)


def stencil(padded, kap, speed_r, speed_p):
    n_r = padded.shape[1] - 4
    n_p = padded.shape[2] - 4

    def tap(a, b):
        return padded[:, 2 + a:2 + a + n_r, 2 + b:2 + b + n_p, :]

    centre = tap(0, 0)
    height = centre.shape[3]
    zpad = jnp.pad(centre, ((0, 0), (0, 0), (0, 0), (2, 2)))

    def ztap(a):
        return zpad[:, :, :, 2 + a:2 + a + height]

    first_r = (tap(-2, 0) - 8.0 * tap(-1, 0) + 8.0 * tap(1, 0) - tap(2, 0)) / 12.0
    first_p = (tap(0, -2) - 8.0 * tap(0, -1) + 8.0 * tap(0, 1) - tap(0, 2)) / 12.0
    second_r = (-tap(-2, 0) + 16.0 * tap(-1, 0) - 30.0 * centre + 16.0 * tap(1, 0) - tap(2, 0)) / 12.0
    second_p = (-tap(0, -2) + 16.0 * tap(0, -1) - 30.0 * centre + 16.0 * tap(0, 1) - tap(0, 2)) / 12.0
    second_z = (-ztap(-2) + 16.0 * ztap(-1) - 30.0 * centre + 16.0 * ztap(1) - ztap(2)) / 12.0
    return (-speed_r[:, :, None, None] * first_r - speed_p[:, :, None, None] * first_p
            + kap[None] * (second_r + second_p + second_z))


def operate(field, kap, speed_r, speed_p):
    padded = jnp.pad(field, ((0, 0), (2, 2), (0, 0), (0, 0)))
    padded = jnp.concatenate([padded[:, :, -2:], padded, padded[:, :, :2]], axis=2)
    return stencil(padded, kap, speed_r, speed_p)


def heun(field, kap, speed_r, speed_p):
    first = field + operate(field, kap, speed_r, speed_p)
    return 0.5 * (field + first + operate(first, kap, speed_r, speed_p))


def one_field(items, kappa, shifts):
    field, speed_r, speed_p = items
    field = field[None]
    speed_r = speed_r[None]
    speed_p = speed_p[None]
    half = heun(field, kappa, speed_r, speed_p)
    count = half.shape[2]
    index = (jnp.arange(count, dtype=jnp.int32)[None, :] - shifts[:, None]) % count
    index = jnp.broadcast_to(index[None, :, :, None], half.shape).astype(jnp.int32)
    moved = jnp.take_along_axis(half, index, axis=2)
    return heun(moved, kappa, speed_r, speed_p)[0]


def reference(fields, kappa, radial_speed, azimuth_speed, shifts):
    return lax.map(lambda items: one_field(items, kappa, shifts), (fields, radial_speed, azimuth_speed))
```

```python
import jax
import jax.numpy as jnp
from jax import lax
from jax.sharding import PartitionSpec as P


def with_halo(cells, sides, width, closed):
    for axis, dim in sides:
        count = lax.axis_size(axis)
        ends = count if closed else count - 1
        head = lax.slice_in_dim(cells, 0, width, axis=dim)
        tail = lax.slice_in_dim(cells, cells.shape[dim] - width, cells.shape[dim], axis=dim)
        cells = jnp.concatenate(
            [
                lax.ppermute(tail, axis, [(i, (i + 1) % count) for i in range(ends)]),
                cells,
                lax.ppermute(head, axis, [((i + 1) % count, i) for i in range(ends)]),
            ],
            axis=dim,
        )
    return cells


def stencil(padded, kap, speed_r, speed_p):
    n_r = padded.shape[1] - 4
    n_p = padded.shape[2] - 4

    def tap(a, b):
        return padded[:, 2 + a : 2 + a + n_r, 2 + b : 2 + b + n_p, :]

    centre = tap(0, 0)
    height = centre.shape[3]
    zpad = jnp.pad(centre, ((0, 0), (0, 0), (0, 0), (2, 2)))

    def ztap(a):
        return zpad[:, :, :, 2 + a : 2 + a + height]

    first_r = (tap(-2, 0) - 8.0 * tap(-1, 0) + 8.0 * tap(1, 0) - tap(2, 0)) / 12.0
    first_p = (tap(0, -2) - 8.0 * tap(0, -1) + 8.0 * tap(0, 1) - tap(0, 2)) / 12.0
    second_r = (
        -tap(-2, 0) + 16.0 * tap(-1, 0) - 30.0 * centre + 16.0 * tap(1, 0) - tap(2, 0)
    ) / 12.0
    second_p = (
        -tap(0, -2) + 16.0 * tap(0, -1) - 30.0 * centre + 16.0 * tap(0, 1) - tap(0, 2)
    ) / 12.0
    second_z = (-ztap(-2) + 16.0 * ztap(-1) - 30.0 * centre + 16.0 * ztap(1) - ztap(2)) / 12.0
    return (
        -speed_r[:, :, None, None] * first_r
        - speed_p[:, :, None, None] * first_p
        + kap[None] * (second_r + second_p + second_z)
    )


def extend(field, width):
    beside_all = with_halo(field, (("azi", 2),), width, True)
    return with_halo(beside_all, (("rad", 1),), width, False)


def heun_sections(field, kappa, speed_r, speed_p):
    first = field + stencil(extend(field, 2), kappa, speed_r, speed_p)
    return 0.5 * (field + first + stencil(extend(first, 2), kappa, speed_r, speed_p))


def shift_rows(half, shifts):
    peers = lax.axis_size("azi")
    rows = half.shape[1]
    per = rows // peers
    full = lax.all_to_all(half, "azi", 1, 2, tiled=True)
    length = full.shape[2]
    first = lax.axis_index("azi") * per
    mine = lax.dynamic_slice_in_dim(shifts, first, per)
    doubled = jnp.concatenate([full, full], axis=2)
    rolled = []
    for row in range(per):
        start = (length - mine[row] % length) % length
        rolled.append(lax.dynamic_slice_in_dim(doubled[:, row], start, length, axis=1))
    moved = jnp.stack(rolled, axis=1)
    return lax.all_to_all(moved, "azi", 2, 1, tiled=True)


def shards(fields, kappa, radial_speed, azimuth_speed, shifts):
    half = heun_sections(fields, kappa, radial_speed, azimuth_speed)
    moved = shift_rows(half, shifts)
    return heun_sections(moved, kappa, radial_speed, azimuth_speed)


def solution(mesh):
    placed = (
        P(None, "rad", "azi", None),
        P("rad", "azi", None),
        P(None, "rad"),
        P(None, "rad"),
        P("rad"),
    )
    return jax.shard_map(
        shards, mesh=mesh, in_specs=placed, out_specs=P(None, "rad", "azi", None), check_vma=False
    )
```

```python
import jax
import jax.numpy as jnp
from jax import lax
from jax.sharding import PartitionSpec as P


def stencil(padded, kap, speed_r, speed_p):
    n_r = padded.shape[1] - 4
    n_p = padded.shape[2] - 4

    def tap(a, b):
        return padded[:, 2 + a : 2 + a + n_r, 2 + b : 2 + b + n_p, :]

    centre = tap(0, 0)
    height = centre.shape[3]
    zpad = jnp.pad(centre, ((0, 0), (0, 0), (0, 0), (2, 2)))

    def ztap(a):
        return zpad[:, :, :, 2 + a : 2 + a + height]

    first_r = (tap(-2, 0) - 8.0 * tap(-1, 0) + 8.0 * tap(1, 0) - tap(2, 0)) / 12.0
    first_p = (tap(0, -2) - 8.0 * tap(0, -1) + 8.0 * tap(0, 1) - tap(0, 2)) / 12.0
    second_r = (
        -tap(-2, 0) + 16.0 * tap(-1, 0) - 30.0 * centre + 16.0 * tap(1, 0) - tap(2, 0)
    ) / 12.0
    second_p = (
        -tap(0, -2) + 16.0 * tap(0, -1) - 30.0 * centre + 16.0 * tap(0, 1) - tap(0, 2)
    ) / 12.0
    second_z = (-ztap(-2) + 16.0 * ztap(-1) - 30.0 * centre + 16.0 * ztap(1) - ztap(2)) / 12.0
    return (
        -speed_r[:, :, None, None] * first_r
        - speed_p[:, :, None, None] * first_p
        + kap[None] * (second_r + second_p + second_z)
    )


def extend(cells, width):
    rings, sectors = lax.axis_size("rad"), lax.axis_size("azi")
    rows, cols = cells.shape[-3], cells.shape[-2]
    spans = {-1: (rows - width, rows), 0: (0, rows), 1: (0, width)}
    cuts = {-1: (cols - width, cols), 0: (0, cols), 1: (0, width)}

    def piece(di, dj):
        block = cells[..., slice(*spans[di]), slice(*cuts[dj]), :]
        pairs = [
            (a * sectors + b, (a - di) * sectors + (b - dj) % sectors)
            for a in range(rings)
            for b in range(sectors)
            if 0 <= a - di < rings
        ]
        return lax.ppermute(block, ("rad", "azi"), pairs)

    bands = []
    for di in (-1, 0, 1):
        parts = [cells if di == dj == 0 else piece(di, dj) for dj in (-1, 0, 1)]
        bands.append(jnp.concatenate(parts, axis=-2))
    return jnp.concatenate(bands, axis=-3)


def radial_halo(values, width):
    rings = lax.axis_size("rad")
    rows = values.shape[-1]
    above = lax.ppermute(values[..., rows - width :], "rad", [(i, i + 1) for i in range(rings - 1)])
    below = lax.ppermute(values[..., :width], "rad", [(i + 1, i) for i in range(rings - 1)])
    return jnp.concatenate([above, values, below], axis=-1)


def heun_sections(field, ext, kap_ext, speed_r, speed_p, inside):
    first = ext[:, 2:-2, 2:-2] + stencil(ext, kap_ext, speed_r, speed_p)
    first = jnp.where(inside[None, :, None, None], first, 0.0)
    kap = kap_ext[2:-2, 2:-2]
    inner = stencil(first, kap, speed_r[:, 2:-2], speed_p[:, 2:-2])
    return 0.5 * (field + first[:, 2:-2, 2:-2] + inner)


def shift_rows(half, shifts):
    peers = lax.axis_size("azi")
    rows = half.shape[1]
    per = rows // peers
    full = lax.all_to_all(half, "azi", 1, 2, tiled=True)
    length = full.shape[2]
    first = lax.axis_index("azi") * per
    mine = lax.dynamic_slice_in_dim(shifts, first, per)
    doubled = jnp.concatenate([full, full], axis=2)
    rolled = []
    for row in range(per):
        start = (length - mine[row] % length) % length
        rolled.append(lax.dynamic_slice_in_dim(doubled[:, row], start, length, axis=1))
    moved = jnp.stack(rolled, axis=1)
    return lax.all_to_all(moved, "azi", 2, 1, tiled=True)


def shards(fields, kappa, radial_speed, azimuth_speed, shifts):
    fcount, rows = fields.shape[0], fields.shape[1]
    joined = extend(jnp.concatenate([fields, kappa[None]], axis=0), 4)
    ext, kap_ext = joined[:fcount], joined[fcount, 2:-2, 2:-2]
    speeds = radial_halo(jnp.stack([radial_speed, azimuth_speed]), 2)
    speed_r, speed_p = speeds[0], speeds[1]
    start = lax.axis_index("rad") * rows - 2
    places = start + jnp.arange(rows + 4)
    inside = (places >= 0) & (places < lax.axis_size("rad") * rows)
    half = heun_sections(fields, ext, kap_ext, speed_r, speed_p, inside)
    moved = shift_rows(half, shifts)
    return heun_sections(moved, extend(moved, 4), kap_ext, speed_r, speed_p, inside)


def solution(mesh):
    placed = (
        P(None, "rad", "azi", None),
        P("rad", "azi", None),
        P(None, "rad"),
        P(None, "rad"),
        P("rad"),
    )
    return jax.shard_map(
        shards, mesh=mesh, in_specs=placed, out_specs=P(None, "rad", "azi", None), check_vma=False
    )
```

```python
import jax
import jax.numpy as jnp
from jax import lax
from jax.sharding import PartitionSpec as P


def stencil(padded, kap, speed_r, speed_p):
    n_r = padded.shape[1] - 4
    n_p = padded.shape[2] - 4

    def tap(a, b):
        return padded[:, 2 + a : 2 + a + n_r, 2 + b : 2 + b + n_p, :]

    centre = tap(0, 0)
    height = centre.shape[3]
    zpad = jnp.pad(centre, ((0, 0), (0, 0), (0, 0), (2, 2)))

    def ztap(a):
        return zpad[:, :, :, 2 + a : 2 + a + height]

    first_r = (tap(-2, 0) - 8.0 * tap(-1, 0) + 8.0 * tap(1, 0) - tap(2, 0)) / 12.0
    first_p = (tap(0, -2) - 8.0 * tap(0, -1) + 8.0 * tap(0, 1) - tap(0, 2)) / 12.0
    second_r = (
        -tap(-2, 0) + 16.0 * tap(-1, 0) - 30.0 * centre + 16.0 * tap(1, 0) - tap(2, 0)
    ) / 12.0
    second_p = (
        -tap(0, -2) + 16.0 * tap(0, -1) - 30.0 * centre + 16.0 * tap(0, 1) - tap(0, 2)
    ) / 12.0
    second_z = (-ztap(-2) + 16.0 * ztap(-1) - 30.0 * centre + 16.0 * ztap(1) - ztap(2)) / 12.0
    return (
        -speed_r[:, :, None, None] * first_r
        - speed_p[:, :, None, None] * first_p
        + kap[None] * (second_r + second_p + second_z)
    )


def extend(cells, width):
    sectors, rings = lax.axis_size("azi"), lax.axis_size("rad")
    rows, cols = cells.shape[-3], cells.shape[-2]
    left = lax.ppermute(cells[..., cols - width :, :], "azi", [(i, (i + 1) % sectors) for i in range(sectors)])
    right = lax.ppermute(cells[..., :width, :], "azi", [((i + 1) % sectors, i) for i in range(sectors)])
    wide = jnp.concatenate([left, cells, right], axis=-2)
    above = lax.ppermute(wide[..., rows - width :, :, :], "rad", [(i, i + 1) for i in range(rings - 1)])
    below = lax.ppermute(wide[..., :width, :, :], "rad", [(i + 1, i) for i in range(rings - 1)])
    return jnp.concatenate([above, wide, below], axis=-3)


def radial_halo(values, width):
    rings = lax.axis_size("rad")
    rows = values.shape[-1]
    above = lax.ppermute(values[..., rows - width :], "rad", [(i, i + 1) for i in range(rings - 1)])
    below = lax.ppermute(values[..., :width], "rad", [(i + 1, i) for i in range(rings - 1)])
    return jnp.concatenate([above, values, below], axis=-1)


def heun_sections(field, ext, kap_ext, speed_r, speed_p, inside):
    first = ext[:, 2:-2, 2:-2] + stencil(ext, kap_ext, speed_r, speed_p)
    first = jnp.where(inside[None, :, None, None], first, 0.0)
    kap = kap_ext[2:-2, 2:-2]
    inner = stencil(first, kap, speed_r[:, 2:-2], speed_p[:, 2:-2])
    return 0.5 * (field + first[:, 2:-2, 2:-2] + inner)


def shift_rows(half, shifts):
    peers = lax.axis_size("azi")
    rows = half.shape[1]
    per = rows // peers
    full = lax.all_to_all(half, "azi", 1, 2, tiled=True)
    length = full.shape[2]
    first = lax.axis_index("azi") * per
    mine = lax.dynamic_slice_in_dim(shifts, first, per)
    doubled = jnp.concatenate([full, full], axis=2)
    rolled = []
    for row in range(per):
        start = (length - mine[row] % length) % length
        rolled.append(lax.dynamic_slice_in_dim(doubled[:, row], start, length, axis=1))
    moved = jnp.stack(rolled, axis=1)
    return lax.all_to_all(moved, "azi", 2, 1, tiled=True)


def shards(fields, kappa, radial_speed, azimuth_speed, shifts):
    fcount, rows = fields.shape[0], fields.shape[1]
    joined = extend(jnp.concatenate([fields, kappa[None]], axis=0), 4)
    ext, kap_ext = joined[:fcount], joined[fcount, 2:-2, 2:-2]
    speeds = radial_halo(jnp.stack([radial_speed, azimuth_speed]), 2)
    speed_r, speed_p = speeds[0], speeds[1]
    start = lax.axis_index("rad") * rows - 2
    places = start + jnp.arange(rows + 4)
    inside = (places >= 0) & (places < lax.axis_size("rad") * rows)
    half = heun_sections(fields, ext, kap_ext, speed_r, speed_p, inside)
    moved = shift_rows(half, shifts)
    return heun_sections(moved, extend(moved, 4), kap_ext, speed_r, speed_p, inside)


def solution(mesh):
    placed = (
        P(None, "rad", "azi", None),
        P("rad", "azi", None),
        P(None, "rad"),
        P(None, "rad"),
        P("rad"),
    )
    return jax.shard_map(
        shards, mesh=mesh, in_specs=placed, out_specs=P(None, "rad", "azi", None), check_vma=False
    )
```

```python
import jax
import jax.numpy as jnp
from jax import lax
from jax.sharding import PartitionSpec as P


def stencil(padded, kap, speed_r, speed_p):
    n_r = padded.shape[1] - 4
    n_p = padded.shape[2] - 4

    def tap(a, b):
        return padded[:, 2 + a : 2 + a + n_r, 2 + b : 2 + b + n_p, :]

    centre = tap(0, 0)
    height = centre.shape[3]
    zpad = jnp.pad(centre, ((0, 0), (0, 0), (0, 0), (2, 2)))

    def ztap(a):
        return zpad[:, :, :, 2 + a : 2 + a + height]

    first_r = (tap(-2, 0) - 8.0 * tap(-1, 0) + 8.0 * tap(1, 0) - tap(2, 0)) / 12.0
    first_p = (tap(0, -2) - 8.0 * tap(0, -1) + 8.0 * tap(0, 1) - tap(0, 2)) / 12.0
    second_r = (
        -tap(-2, 0) + 16.0 * tap(-1, 0) - 30.0 * centre + 16.0 * tap(1, 0) - tap(2, 0)
    ) / 12.0
    second_p = (
        -tap(0, -2) + 16.0 * tap(0, -1) - 30.0 * centre + 16.0 * tap(0, 1) - tap(0, 2)
    ) / 12.0
    second_z = (-ztap(-2) + 16.0 * ztap(-1) - 30.0 * centre + 16.0 * ztap(1) - ztap(2)) / 12.0
    return (
        -speed_r[:, :, None, None] * first_r
        - speed_p[:, :, None, None] * first_p
        + kap[None] * (second_r + second_p + second_z)
    )


def extend(cells, width):
    sectors, rings = lax.axis_size("azi"), lax.axis_size("rad")
    rows, cols = cells.shape[-3], cells.shape[-2]
    left = lax.ppermute(cells[..., cols - width :, :], "azi", [(i, (i + 1) % sectors) for i in range(sectors)])
    right = lax.ppermute(cells[..., :width, :], "azi", [((i + 1) % sectors, i) for i in range(sectors)])
    above = lax.ppermute(cells[..., rows - width :, :, :], "rad", [(i, i + 1) for i in range(rings - 1)])
    below = lax.ppermute(cells[..., :width, :, :], "rad", [(i + 1, i) for i in range(rings - 1)])
    wide = jnp.concatenate([left, cells, right], axis=-2)
    corners = [(0, 0)] * (cells.ndim - 2) + [(width, width), (0, 0)]
    return jnp.concatenate([jnp.pad(above, corners), wide, jnp.pad(below, corners)], axis=-3)


def heun_sections(field, kappa, speed_r, speed_p):
    first = field + stencil(extend(field, 2), kappa, speed_r, speed_p)
    return 0.5 * (field + first + stencil(extend(first, 2), kappa, speed_r, speed_p))


def shift_rows(half, shifts):
    peers = lax.axis_size("azi")
    rows = half.shape[1]
    per = rows // peers
    full = lax.all_to_all(half, "azi", 1, 2, tiled=True)
    length = full.shape[2]
    first = lax.axis_index("azi") * per
    mine = lax.dynamic_slice_in_dim(shifts, first, per)
    doubled = jnp.concatenate([full, full], axis=2)
    rolled = []
    for row in range(per):
        start = (length - mine[row] % length) % length
        rolled.append(lax.dynamic_slice_in_dim(doubled[:, row], start, length, axis=1))
    moved = jnp.stack(rolled, axis=1)
    return lax.all_to_all(moved, "azi", 2, 1, tiled=True)


def shards(fields, kappa, radial_speed, azimuth_speed, shifts):
    half = heun_sections(fields, kappa, radial_speed, azimuth_speed)
    moved = shift_rows(half, shifts)
    return heun_sections(moved, kappa, radial_speed, azimuth_speed)


def solution(mesh):
    placed = (
        P(None, "rad", "azi", None),
        P("rad", "azi", None),
        P(None, "rad"),
        P(None, "rad"),
        P("rad"),
    )
    return jax.shard_map(
        shards, mesh=mesh, in_specs=placed, out_specs=P(None, "rad", "azi", None), check_vma=False
    )
```

```python
import jax
import jax.numpy as jnp
from jax import lax
from jax.sharding import PartitionSpec as P


def stencil(padded, kap, speed_r, speed_p):
    n_r = padded.shape[1] - 4
    n_p = padded.shape[2] - 4

    def tap(a, b):
        return padded[:, 2 + a : 2 + a + n_r, 2 + b : 2 + b + n_p, :]

    centre = tap(0, 0)
    height = centre.shape[3]
    zpad = jnp.pad(centre, ((0, 0), (0, 0), (0, 0), (2, 2)))

    def ztap(a):
        return zpad[:, :, :, 2 + a : 2 + a + height]

    first_r = (tap(-2, 0) - 8.0 * tap(-1, 0) + 8.0 * tap(1, 0) - tap(2, 0)) / 12.0
    first_p = (tap(0, -2) - 8.0 * tap(0, -1) + 8.0 * tap(0, 1) - tap(0, 2)) / 12.0
    second_r = (
        -tap(-2, 0) + 16.0 * tap(-1, 0) - 30.0 * centre + 16.0 * tap(1, 0) - tap(2, 0)
    ) / 12.0
    second_p = (
        -tap(0, -2) + 16.0 * tap(0, -1) - 30.0 * centre + 16.0 * tap(0, 1) - tap(0, 2)
    ) / 12.0
    second_z = (-ztap(-2) + 16.0 * ztap(-1) - 30.0 * centre + 16.0 * ztap(1) - ztap(2)) / 12.0
    return (
        -speed_r[:, :, None, None] * first_r
        - speed_p[:, :, None, None] * first_p
        + kap[None] * (second_r + second_p + second_z)
    )


def extend(cells, width):
    sectors, rings = lax.axis_size("azi"), lax.axis_size("rad")
    rows, cols = cells.shape[-3], cells.shape[-2]
    left = lax.ppermute(cells[..., cols - width :, :], "azi", [(i, (i + 1) % sectors) for i in range(sectors)])
    right = lax.ppermute(cells[..., :width, :], "azi", [((i + 1) % sectors, i) for i in range(sectors)])
    above = lax.ppermute(cells[..., rows - width :, :, :], "rad", [(i, i + 1) for i in range(rings - 1)])
    below = lax.ppermute(cells[..., :width, :, :], "rad", [(i + 1, i) for i in range(rings - 1)])
    wide = jnp.concatenate([left, cells, right], axis=-2)
    corners = [(0, 0)] * (cells.ndim - 2) + [(width, width), (0, 0)]
    return jnp.concatenate([jnp.pad(above, corners), wide, jnp.pad(below, corners)], axis=-3)


def heun_sections(field, kappa, speed_r, speed_p):
    first = field + stencil(extend(field, 2), kappa, speed_r, speed_p)
    return 0.5 * (field + first + stencil(extend(first, 2), kappa, speed_r, speed_p))


def shift_rows(half, shifts):
    peers = lax.axis_size("azi")
    rows = half.shape[1]
    per = rows // peers
    full = lax.all_to_all(half, "azi", 1, 2, tiled=True)
    length = full.shape[2]
    first = lax.axis_index("azi") * per
    mine = lax.dynamic_slice_in_dim(shifts, first, per)
    doubled = jnp.concatenate([full, full], axis=2)
    rolled = []
    for row in range(per):
        start = (length - mine[row] % length) % length
        rolled.append(lax.dynamic_slice_in_dim(doubled[:, row], start, length, axis=1))
    moved = jnp.stack(rolled, axis=1)
    return lax.all_to_all(moved, "azi", 2, 1, tiled=True)


def shards(fields, kappa, radial_speed, azimuth_speed, shifts):
    fcount = fields.shape[0]
    bounds = [0, (fcount + 1) // 2, fcount]
    groups = [(fields[lo:hi], radial_speed[lo:hi], azimuth_speed[lo:hi]) for lo, hi in zip(bounds, bounds[1:])]
    halves = [heun_sections(f, kappa, r, p) for f, r, p in groups]
    moved = [shift_rows(h, shifts) for h in halves]
    done = [heun_sections(m, kappa, r, p) for m, (_, r, p) in zip(moved, groups)]
    return jnp.concatenate(done, axis=0)


def solution(mesh):
    placed = (
        P(None, "rad", "azi", None),
        P("rad", "azi", None),
        P(None, "rad"),
        P(None, "rad"),
        P("rad"),
    )
    return jax.shard_map(
        shards, mesh=mesh, in_specs=placed, out_specs=P(None, "rad", "azi", None), check_vma=False
    )
```

```python
import jax
import jax.numpy as jnp
from jax import lax
from jax.sharding import PartitionSpec as P


def stencil(padded, kap, speed_r, speed_p):
    n_r = padded.shape[1] - 4
    n_p = padded.shape[2] - 4

    def tap(a, b):
        return padded[:, 2 + a : 2 + a + n_r, 2 + b : 2 + b + n_p, :]

    centre = tap(0, 0)
    height = centre.shape[3]
    zpad = jnp.pad(centre, ((0, 0), (0, 0), (0, 0), (2, 2)))

    def ztap(a):
        return zpad[:, :, :, 2 + a : 2 + a + height]

    first_r = (tap(-2, 0) - 8.0 * tap(-1, 0) + 8.0 * tap(1, 0) - tap(2, 0)) / 12.0
    first_p = (tap(0, -2) - 8.0 * tap(0, -1) + 8.0 * tap(0, 1) - tap(0, 2)) / 12.0
    second_r = (
        -tap(-2, 0) + 16.0 * tap(-1, 0) - 30.0 * centre + 16.0 * tap(1, 0) - tap(2, 0)
    ) / 12.0
    second_p = (
        -tap(0, -2) + 16.0 * tap(0, -1) - 30.0 * centre + 16.0 * tap(0, 1) - tap(0, 2)
    ) / 12.0
    second_z = (-ztap(-2) + 16.0 * ztap(-1) - 30.0 * centre + 16.0 * ztap(1) - ztap(2)) / 12.0
    return (
        -speed_r[:, :, None, None] * first_r
        - speed_p[:, :, None, None] * first_p
        + kap[None] * (second_r + second_p + second_z)
    )


def split_stencil(cells, kap, speed_r, speed_p, width=2):
    sectors, rings = lax.axis_size("azi"), lax.axis_size("rad")
    rows, cols = cells.shape[-3], cells.shape[-2]
    left = lax.ppermute(cells[..., cols - width :, :], "azi", [(i, (i + 1) % sectors) for i in range(sectors)])
    right = lax.ppermute(cells[..., :width, :], "azi", [((i + 1) % sectors, i) for i in range(sectors)])
    above = lax.ppermute(cells[..., rows - width :, :, :], "rad", [(i, i + 1) for i in range(rings - 1)])
    below = lax.ppermute(cells[..., :width, :, :], "rad", [(i + 1, i) for i in range(rings - 1)])
    middle = stencil(jnp.concatenate([above, cells, below], axis=1), kap[:, width : cols - width], speed_r, speed_p)
    edge = 2 * width

    def side(strip, near, far, pads):
        wide = jnp.concatenate([strip, near] if pads[0] else [near, strip], axis=2)
        corners = [(0, 0), (0, 0), pads, (0, 0)]
        tall = jnp.concatenate([jnp.pad(far[0], corners), wide, jnp.pad(far[1], corners)], axis=1)
        return tall

    low = side(left, cells[:, :, :edge], (above[:, :, :edge], below[:, :, :edge]), (width, 0))
    high = side(right, cells[:, :, cols - edge :], (above[:, :, cols - edge :], below[:, :, cols - edge :]), (0, width))
    first = stencil(low, kap[:, :width], speed_r, speed_p)
    last = stencil(high, kap[:, cols - width :], speed_r, speed_p)
    return jnp.concatenate([first, middle, last], axis=2)


def heun_sections(field, kappa, speed_r, speed_p):
    first = field + split_stencil(field, kappa, speed_r, speed_p)
    return 0.5 * (field + first + split_stencil(first, kappa, speed_r, speed_p))


def shift_rows(half, shifts):
    peers = lax.axis_size("azi")
    rows = half.shape[1]
    per = rows // peers
    full = lax.all_to_all(half, "azi", 1, 2, tiled=True)
    length = full.shape[2]
    first = lax.axis_index("azi") * per
    mine = lax.dynamic_slice_in_dim(shifts, first, per)
    doubled = jnp.concatenate([full, full], axis=2)
    rolled = []
    for row in range(per):
        start = (length - mine[row] % length) % length
        rolled.append(lax.dynamic_slice_in_dim(doubled[:, row], start, length, axis=1))
    moved = jnp.stack(rolled, axis=1)
    return lax.all_to_all(moved, "azi", 2, 1, tiled=True)


def shards(fields, kappa, radial_speed, azimuth_speed, shifts):
    half = heun_sections(fields, kappa, radial_speed, azimuth_speed)
    moved = shift_rows(half, shifts)
    return heun_sections(moved, kappa, radial_speed, azimuth_speed)


def solution(mesh):
    placed = (
        P(None, "rad", "azi", None),
        P("rad", "azi", None),
        P(None, "rad"),
        P(None, "rad"),
        P("rad"),
    )
    return jax.shard_map(
        shards, mesh=mesh, in_specs=placed, out_specs=P(None, "rad", "azi", None), check_vma=False
    )
```

```python
import jax
import jax.numpy as jnp
from jax import lax
from jax.sharding import PartitionSpec as P
from jax.experimental.layout import Layout, with_layout_constraint


def stencil(padded, kap, speed_r, speed_p):
    n_r = padded.shape[1] - 4
    n_p = padded.shape[2] - 4

    def tap(a, b):
        return padded[:, 2 + a : 2 + a + n_r, 2 + b : 2 + b + n_p, :]

    centre = tap(0, 0)
    height = centre.shape[3]
    zpad = jnp.pad(centre, ((0, 0), (0, 0), (0, 0), (2, 2)))

    def ztap(a):
        return zpad[:, :, :, 2 + a : 2 + a + height]

    first_r = (tap(-2, 0) - 8.0 * tap(-1, 0) + 8.0 * tap(1, 0) - tap(2, 0)) / 12.0
    first_p = (tap(0, -2) - 8.0 * tap(0, -1) + 8.0 * tap(0, 1) - tap(0, 2)) / 12.0
    second_r = (
        -tap(-2, 0) + 16.0 * tap(-1, 0) - 30.0 * centre + 16.0 * tap(1, 0) - tap(2, 0)
    ) / 12.0
    second_p = (
        -tap(0, -2) + 16.0 * tap(0, -1) - 30.0 * centre + 16.0 * tap(0, 1) - tap(0, 2)
    ) / 12.0
    second_z = (-ztap(-2) + 16.0 * ztap(-1) - 30.0 * centre + 16.0 * ztap(1) - ztap(2)) / 12.0
    return (
        -speed_r[:, :, None, None] * first_r
        - speed_p[:, :, None, None] * first_p
        + kap[None] * (second_r + second_p + second_z)
    )


def split_stencil(cells, kap, speed_r, speed_p, width=2):
    sectors, rings = lax.axis_size("azi"), lax.axis_size("rad")
    rows, cols = cells.shape[-3], cells.shape[-2]
    left = lax.ppermute(cells[..., cols - width :, :], "azi", [(i, (i + 1) % sectors) for i in range(sectors)])
    right = lax.ppermute(cells[..., :width, :], "azi", [((i + 1) % sectors, i) for i in range(sectors)])
    above = lax.ppermute(cells[..., rows - width :, :, :], "rad", [(i, i + 1) for i in range(rings - 1)])
    below = lax.ppermute(cells[..., :width, :, :], "rad", [(i + 1, i) for i in range(rings - 1)])
    middle = stencil(jnp.concatenate([above, cells, below], axis=1), kap[:, width : cols - width], speed_r, speed_p)
    edge = 2 * width

    def side(strip, near, far, pads):
        wide = jnp.concatenate([strip, near] if pads[0] else [near, strip], axis=2)
        corners = [(0, 0), (0, 0), pads, (0, 0)]
        tall = jnp.concatenate([jnp.pad(far[0], corners), wide, jnp.pad(far[1], corners)], axis=1)
        return tall

    low = side(left, cells[:, :, :edge], (above[:, :, :edge], below[:, :, :edge]), (width, 0))
    high = side(right, cells[:, :, cols - edge :], (above[:, :, cols - edge :], below[:, :, cols - edge :]), (0, width))
    first = stencil(low, kap[:, :width], speed_r, speed_p)
    last = stencil(high, kap[:, cols - width :], speed_r, speed_p)
    return jnp.concatenate([first, middle, last], axis=2)


def heun_sections(field, kappa, speed_r, speed_p):
    first = field + split_stencil(field, kappa, speed_r, speed_p)
    return 0.5 * (field + first + split_stencil(first, kappa, speed_r, speed_p))


def shift_rows(half, shifts):
    peers = lax.axis_size("azi")
    rows = half.shape[1]
    per = rows // peers
    full = lax.all_to_all(half, "azi", 1, 2, tiled=True)
    length = full.shape[2]
    first = lax.axis_index("azi") * per
    mine = lax.dynamic_slice_in_dim(shifts, first, per)
    doubled = jnp.concatenate([full, full], axis=2)
    rolled = []
    for row in range(per):
        start = (length - mine[row] % length) % length
        rolled.append(lax.dynamic_slice_in_dim(doubled[:, row], start, length, axis=1))
    moved = jnp.stack(rolled, axis=1)
    return lax.all_to_all(moved, "azi", 2, 1, tiled=True)


def shards(fields, kappa, radial_speed, azimuth_speed, shifts):
    half = with_layout_constraint(heun_sections(fields, kappa, radial_speed, azimuth_speed), Layout((1, 0, 2, 3)))
    moved = shift_rows(half, shifts)
    return with_layout_constraint(heun_sections(moved, kappa, radial_speed, azimuth_speed), Layout((0, 1, 2, 3)))


def solution(mesh):
    placed = (
        P(None, "rad", "azi", None),
        P("rad", "azi", None),
        P(None, "rad"),
        P(None, "rad"),
        P("rad"),
    )
    return jax.shard_map(
        shards, mesh=mesh, in_specs=placed, out_specs=P(None, "rad", "azi", None), check_vma=False
    )
```

```python
import jax
import jax.numpy as jnp
from jax import lax
from jax.sharding import PartitionSpec as P


def stencil(padded, kap, speed_r, speed_p):
    n_r = padded.shape[1] - 4
    n_p = padded.shape[2] - 4

    def tap(a, b):
        return padded[:, 2 + a : 2 + a + n_r, 2 + b : 2 + b + n_p, :]

    centre = tap(0, 0)
    height = centre.shape[3]
    zpad = jnp.pad(centre, ((0, 0), (0, 0), (0, 0), (2, 2)))

    def ztap(a):
        return zpad[:, :, :, 2 + a : 2 + a + height]

    first_r = (tap(-2, 0) - 8.0 * tap(-1, 0) + 8.0 * tap(1, 0) - tap(2, 0)) / 12.0
    first_p = (tap(0, -2) - 8.0 * tap(0, -1) + 8.0 * tap(0, 1) - tap(0, 2)) / 12.0
    second_r = (
        -tap(-2, 0) + 16.0 * tap(-1, 0) - 30.0 * centre + 16.0 * tap(1, 0) - tap(2, 0)
    ) / 12.0
    second_p = (
        -tap(0, -2) + 16.0 * tap(0, -1) - 30.0 * centre + 16.0 * tap(0, 1) - tap(0, 2)
    ) / 12.0
    second_z = (-ztap(-2) + 16.0 * ztap(-1) - 30.0 * centre + 16.0 * ztap(1) - ztap(2)) / 12.0
    return (
        -speed_r[:, :, None, None] * first_r
        - speed_p[:, :, None, None] * first_p
        + kap[None] * (second_r + second_p + second_z)
    )


def shifted(cells, axis, by, closed):
    peers = lax.axis_size(axis)
    ends = peers if closed else peers - 1
    if by > 0:
        return lax.ppermute(cells, axis, [(i, (i + 1) % peers) for i in range(ends)])
    return lax.ppermute(cells, axis, [((i + 1) % peers, i) for i in range(ends)])


def fringe(strip, cols):
    return jnp.pad(strip, [(0, 0), (0, 0), (cols, cols), (0, 0)])


def heun_sections(field, kap_wide, speed_r, speed_p, kap_strips=None):
    fcount, rows, cols = field.shape[0], field.shape[1], field.shape[2]
    sides = (field[:, :, cols - 4 :], field[:, :, :4])
    if kap_strips is not None:
        sides = tuple(jnp.concatenate([s, k[None]], axis=0) for s, k in zip(sides, kap_strips))
    left = shifted(sides[0], "azi", 1, True)
    right = shifted(sides[1], "azi", -1, True)
    above = shifted(field[:, rows - 2 :], "rad", 1, False)
    below = shifted(field[:, :2], "rad", -1, False)
    if kap_strips is not None:
        kap_wide = jnp.concatenate([left[fcount, :, 2:], kap_wide, right[fcount, :, :2]], axis=1)
        left, right = left[:fcount], right[:fcount]
    wide = jnp.concatenate([left, field, right], axis=2)
    grown = jnp.concatenate([fringe(above, 4), wide, fringe(below, 4)], axis=1)
    first = wide[:, :, 2:-2] + stencil(grown, kap_wide, speed_r, speed_p)

    def corners(part):
        return jnp.concatenate([part[:, :, 2:4], part[:, :, cols + 4 : cols + 6]], axis=2)

    up = jnp.concatenate([first[:, rows - 2 :, 2 : cols + 2], corners(wide[:, rows - 2 :])], axis=2)
    down = jnp.concatenate([first[:, :2, 2 : cols + 2], corners(wide[:, :2])], axis=2)
    top = shifted(up, "rad", 1, False)
    bottom = shifted(down, "rad", -1, False)

    fixes = []
    for side_rows, halo, outer in ((slice(0, 2), top, True), (slice(rows - 2, rows), bottom, False)):
        for lo, cstart in ((cols, 0), (cols + 2, cols + 2)):
            near = grown[:, 2:6] if outer else grown[:, rows - 2 : rows + 2]
            near = near[:, :, cstart : cstart + 6]
            block = jnp.zeros((fcount, 2, 6, field.shape[3]), field.dtype)
            block = block.at[:, :, 2:4].set(halo[:, :, lo : lo + 2])
            tile = jnp.concatenate([block, near] if outer else [near, block], axis=1)
            out_rows = slice(0, 2) if outer else slice(rows - 2, rows)
            kap = kap_wide[out_rows, cstart : cstart + 2]
            base = wide[:, out_rows, cstart + 2 : cstart + 4]
            fixes.append((out_rows, cstart, base + stencil(tile, kap, speed_r[:, out_rows], speed_p[:, out_rows])))
    for out_rows, cstart, value in fixes:
        first = first.at[:, out_rows, cstart : cstart + 2].set(value)
    tall = jnp.concatenate([fringe(top[:, :, :cols], 2), first, fringe(bottom[:, :, :cols], 2)], axis=1)
    inner = stencil(tall, kap_wide[:, 2:-2], speed_r, speed_p)
    return 0.5 * (field + first[:, :, 2:-2] + inner), kap_wide


def shift_rows(half, shifts):
    peers = lax.axis_size("azi")
    rows = half.shape[1]
    per = rows // peers
    full = lax.all_to_all(half, "azi", 1, 2, tiled=True)
    length = full.shape[2]
    first = lax.axis_index("azi") * per
    mine = lax.dynamic_slice_in_dim(shifts, first, per)
    doubled = jnp.concatenate([full, full], axis=2)
    rolled = []
    for row in range(per):
        start = (length - mine[row] % length) % length
        rolled.append(lax.dynamic_slice_in_dim(doubled[:, row], start, length, axis=1))
    moved = jnp.stack(rolled, axis=1)
    return lax.all_to_all(moved, "azi", 2, 1, tiled=True)


def shards(fields, kappa, radial_speed, azimuth_speed, shifts):
    cols = kappa.shape[1]
    strips = (kappa[:, cols - 4 :], kappa[:, :4])
    half, kap_wide = heun_sections(fields, kappa, radial_speed, azimuth_speed, strips)
    moved = shift_rows(half, shifts)
    return heun_sections(moved, kap_wide, radial_speed, azimuth_speed)[0]


def solution(mesh):
    placed = (
        P(None, "rad", "azi", None),
        P("rad", "azi", None),
        P(None, "rad"),
        P(None, "rad"),
        P("rad"),
    )
    return jax.shard_map(
        shards, mesh=mesh, in_specs=placed, out_specs=P(None, "rad", "azi", None), check_vma=False
    )
```

```python
import jax
import jax.numpy as jnp
from jax import lax
from jax.sharding import PartitionSpec as P


def stencil(padded, kap, speed_r, speed_p):
    n_r = padded.shape[1] - 4
    n_p = padded.shape[2] - 4

    def tap(a, b):
        return padded[:, 2 + a : 2 + a + n_r, 2 + b : 2 + b + n_p, :]

    centre = tap(0, 0)
    height = centre.shape[3]
    zpad = jnp.pad(centre, ((0, 0), (0, 0), (0, 0), (2, 2)))

    def ztap(a):
        return zpad[:, :, :, 2 + a : 2 + a + height]

    first_r = (tap(-2, 0) - 8.0 * tap(-1, 0) + 8.0 * tap(1, 0) - tap(2, 0)) / 12.0
    first_p = (tap(0, -2) - 8.0 * tap(0, -1) + 8.0 * tap(0, 1) - tap(0, 2)) / 12.0
    second_r = (
        -tap(-2, 0) + 16.0 * tap(-1, 0) - 30.0 * centre + 16.0 * tap(1, 0) - tap(2, 0)
    ) / 12.0
    second_p = (
        -tap(0, -2) + 16.0 * tap(0, -1) - 30.0 * centre + 16.0 * tap(0, 1) - tap(0, 2)
    ) / 12.0
    second_z = (-ztap(-2) + 16.0 * ztap(-1) - 30.0 * centre + 16.0 * ztap(1) - ztap(2)) / 12.0
    return (
        -speed_r[:, :, None, None] * first_r
        - speed_p[:, :, None, None] * first_p
        + kap[None] * (second_r + second_p + second_z)
    )


def shifted(cells, axis, by, closed):
    peers = lax.axis_size(axis)
    ends = peers if closed else peers - 1
    if by > 0:
        return lax.ppermute(cells, axis, [(i, (i + 1) % peers) for i in range(ends)])
    return lax.ppermute(cells, axis, [((i + 1) % peers, i) for i in range(ends)])


def fringe(strip, cols):
    return jnp.pad(strip, [(0, 0), (0, 0), (cols, cols), (0, 0)])


def heun_sections(field, kap_wide, speed_r, speed_p, kap_strips=None):
    fcount, rows, cols = field.shape[0], field.shape[1], field.shape[2]
    sides = (field[:, :, cols - 4 :], field[:, :, :4])
    if kap_strips is not None:
        sides = tuple(jnp.concatenate([s, k[None]], axis=0) for s, k in zip(sides, kap_strips))
    left = shifted(sides[0], "azi", 1, True)
    right = shifted(sides[1], "azi", -1, True)
    above = shifted(field[:, rows - 2 :], "rad", 1, False)
    below = shifted(field[:, :2], "rad", -1, False)
    if kap_strips is not None:
        kap_wide = jnp.concatenate([left[fcount, :, 2:], kap_wide, right[fcount, :, :2]], axis=1)
        left, right = left[:fcount], right[:fcount]
    wide = jnp.concatenate([left, field, right], axis=2)
    grown = jnp.concatenate([fringe(above, 4), wide, fringe(below, 4)], axis=1)
    first = wide[:, :, 2:-2] + stencil(grown, kap_wide, speed_r, speed_p)

    def corners(part):
        return jnp.concatenate([part[:, :, 2:4], part[:, :, cols + 4 : cols + 6]], axis=2)

    up = jnp.concatenate([first[:, rows - 2 :, 2 : cols + 2], corners(wide[:, rows - 2 :])], axis=2)
    down = jnp.concatenate([first[:, :2, 2 : cols + 2], corners(wide[:, :2])], axis=2)
    top = shifted(up, "rad", 1, False)
    bottom = shifted(down, "rad", -1, False)

    tiles, kaps, rates, turns, bases = [], [], [], [], []
    for halo, outer in ((top, True), (bottom, False)):
        out_rows = slice(0, 2) if outer else slice(rows - 2, rows)
        for lo, cstart in ((cols, 0), (cols + 2, cols + 2)):
            near = grown[:, 2:6] if outer else grown[:, rows - 2 : rows + 2]
            near = near[:, :, cstart : cstart + 6]
            block = jnp.pad(halo[:, :, lo : lo + 2], [(0, 0), (0, 0), (2, 2), (0, 0)])
            tiles.append(jnp.concatenate([block, near] if outer else [near, block], axis=1))
            kaps.append(kap_wide[out_rows, cstart : cstart + 2])
            rates.append(speed_r[:, out_rows])
            turns.append(speed_p[:, out_rows])
            bases.append(wide[:, out_rows, cstart + 2 : cstart + 4])
    fixed = jnp.stack(bases) + jax.vmap(stencil)(jnp.stack(tiles), jnp.stack(kaps), jnp.stack(rates), jnp.stack(turns))
    gap = jnp.zeros((fcount, 2, cols, field.shape[3]), field.dtype)
    bands = [jnp.concatenate([fixed[2 * k], gap, fixed[2 * k + 1]], axis=2) for k in (0, 1)]
    middle = jnp.zeros((fcount, rows - 4, cols + 4, field.shape[3]), field.dtype)
    patches = jnp.concatenate([bands[0], middle, bands[1]], axis=1)
    row_at = lax.broadcasted_iota(jnp.int32, (rows, cols + 4), 0)
    col_at = lax.broadcasted_iota(jnp.int32, (rows, cols + 4), 1)
    edge_rows = (row_at < 2) | (row_at >= rows - 2)
    edge_cols = (col_at < 2) | (col_at >= cols + 2)
    first = jnp.where((edge_rows & edge_cols)[None, :, :, None], patches, first)
    tall = jnp.concatenate([fringe(top[:, :, :cols], 2), first, fringe(bottom[:, :, :cols], 2)], axis=1)
    inner = stencil(tall, kap_wide[:, 2:-2], speed_r, speed_p)
    return 0.5 * (field + first[:, :, 2:-2] + inner), kap_wide


def shift_rows(half, shifts):
    peers = lax.axis_size("azi")
    rows = half.shape[1]
    per = rows // peers
    full = lax.all_to_all(half, "azi", 1, 2, tiled=True)
    length = full.shape[2]
    first = lax.axis_index("azi") * per
    mine = lax.dynamic_slice_in_dim(shifts, first, per)
    doubled = jnp.concatenate([full, full], axis=2)
    rolled = []
    for row in range(per):
        start = (length - mine[row] % length) % length
        rolled.append(lax.dynamic_slice_in_dim(doubled[:, row], start, length, axis=1))
    moved = jnp.stack(rolled, axis=1)
    return lax.all_to_all(moved, "azi", 2, 1, tiled=True)


def shards(fields, kappa, radial_speed, azimuth_speed, shifts):
    cols = kappa.shape[1]
    strips = (kappa[:, cols - 4 :], kappa[:, :4])
    half, kap_wide = heun_sections(fields, kappa, radial_speed, azimuth_speed, strips)
    moved = shift_rows(half, shifts)
    return heun_sections(moved, kap_wide, radial_speed, azimuth_speed)[0]


def solution(mesh):
    placed = (
        P(None, "rad", "azi", None),
        P("rad", "azi", None),
        P(None, "rad"),
        P(None, "rad"),
        P("rad"),
    )
    return jax.shard_map(
        shards, mesh=mesh, in_specs=placed, out_specs=P(None, "rad", "azi", None), check_vma=False
    )
```

```python
import jax
import jax.numpy as jnp
from jax import lax
from jax.sharding import PartitionSpec as P


def stencil(padded, kap, speed_r, speed_p):
    n_r = padded.shape[1] - 4
    n_p = padded.shape[2] - 4

    def tap(a, b):
        return padded[:, 2 + a : 2 + a + n_r, 2 + b : 2 + b + n_p, :]

    centre = tap(0, 0)
    height = centre.shape[3]
    zpad = jnp.pad(centre, ((0, 0), (0, 0), (0, 0), (2, 2)))

    def ztap(a):
        return zpad[:, :, :, 2 + a : 2 + a + height]

    first_r = (tap(-2, 0) - 8.0 * tap(-1, 0) + 8.0 * tap(1, 0) - tap(2, 0)) / 12.0
    first_p = (tap(0, -2) - 8.0 * tap(0, -1) + 8.0 * tap(0, 1) - tap(0, 2)) / 12.0
    second_r = (
        -tap(-2, 0) + 16.0 * tap(-1, 0) - 30.0 * centre + 16.0 * tap(1, 0) - tap(2, 0)
    ) / 12.0
    second_p = (
        -tap(0, -2) + 16.0 * tap(0, -1) - 30.0 * centre + 16.0 * tap(0, 1) - tap(0, 2)
    ) / 12.0
    second_z = (-ztap(-2) + 16.0 * ztap(-1) - 30.0 * centre + 16.0 * ztap(1) - ztap(2)) / 12.0
    return (
        -speed_r[:, :, None, None] * first_r
        - speed_p[:, :, None, None] * first_p
        + kap[None] * (second_r + second_p + second_z)
    )


def split_stencil(cells, kap, speed_r, speed_p, width=2):
    sectors, rings = lax.axis_size("azi"), lax.axis_size("rad")
    rows, cols = cells.shape[-3], cells.shape[-2]
    left = lax.ppermute(cells[..., cols - width :, :], "azi", [(i, (i + 1) % sectors) for i in range(sectors)])
    right = lax.ppermute(cells[..., :width, :], "azi", [((i + 1) % sectors, i) for i in range(sectors)])
    above = lax.ppermute(cells[..., rows - width :, :, :], "rad", [(i, i + 1) for i in range(rings - 1)])
    below = lax.ppermute(cells[..., :width, :, :], "rad", [(i + 1, i) for i in range(rings - 1)])
    middle = stencil(jnp.concatenate([above, cells, below], axis=1), kap[:, width : cols - width], speed_r, speed_p)
    edge = 2 * width

    def side(strip, near, far, pads):
        wide = jnp.concatenate([strip, near] if pads[0] else [near, strip], axis=2)
        corners = [(0, 0), (0, 0), pads, (0, 0)]
        tall = jnp.concatenate([jnp.pad(far[0], corners), wide, jnp.pad(far[1], corners)], axis=1)
        return tall

    low = side(left, cells[:, :, :edge], (above[:, :, :edge], below[:, :, :edge]), (width, 0))
    high = side(right, cells[:, :, cols - edge :], (above[:, :, cols - edge :], below[:, :, cols - edge :]), (0, width))
    first = stencil(low, kap[:, :width], speed_r, speed_p)
    last = stencil(high, kap[:, cols - width :], speed_r, speed_p)
    return jnp.concatenate([first, middle, last], axis=2)


def heun_sections(field, kappa, speed_r, speed_p):
    first = field + split_stencil(field, kappa, speed_r, speed_p)
    return 0.5 * (field + first + split_stencil(first, kappa, speed_r, speed_p))


def shift_rows(half, shifts, width=2):
    peers = lax.axis_size("azi")
    fcount, rows, cols, height = half.shape
    per = rows // peers
    full = lax.all_to_all(half, "azi", 1, 2, tiled=True)
    length = full.shape[2]
    first = lax.axis_index("azi") * per
    mine = lax.dynamic_slice_in_dim(shifts, first, per)
    doubled = jnp.concatenate([full, full], axis=2)
    rolled = []
    for row in range(per):
        start = (length - mine[row] % length) % length
        rolled.append(lax.dynamic_slice_in_dim(doubled[:, row], start, length, axis=1))
    moved = jnp.stack(rolled, axis=1)
    ring = jnp.concatenate([moved[:, :, length - width :], moved, moved[:, :, :width]], axis=2)
    windows = jnp.stack([ring[:, :, k * cols : k * cols + cols + 2 * width] for k in range(peers)])
    back = lax.all_to_all(windows, "azi", 0, 0)
    return jnp.moveaxis(back, 0, 1).reshape(fcount, rows, cols + 2 * width, height)


def shards(fields, kappa, radial_speed, azimuth_speed, shifts):
    half = heun_sections(fields, kappa, radial_speed, azimuth_speed)
    wide = shift_rows(half, shifts)
    moved = wide[:, :, 2:-2]
    rows = moved.shape[1]
    above = lax.ppermute(moved[:, rows - 2 :], "rad", [(i, i + 1) for i in range(lax.axis_size("rad") - 1)])
    below = lax.ppermute(moved[:, :2], "rad", [(i + 1, i) for i in range(lax.axis_size("rad") - 1)])
    corners = [(0, 0), (0, 0), (2, 2), (0, 0)]
    padded = jnp.concatenate([jnp.pad(above, corners), wide, jnp.pad(below, corners)], axis=1)
    first = moved + stencil(padded, kappa, radial_speed, azimuth_speed)
    inner = split_stencil(first, kappa, radial_speed, azimuth_speed)
    return 0.5 * (moved + first + inner)


def solution(mesh):
    placed = (
        P(None, "rad", "azi", None),
        P("rad", "azi", None),
        P(None, "rad"),
        P(None, "rad"),
        P("rad"),
    )
    return jax.shard_map(
        shards, mesh=mesh, in_specs=placed, out_specs=P(None, "rad", "azi", None), check_vma=False
    )
```

```python
import jax
import jax.numpy as jnp
from jax import lax
from jax.sharding import PartitionSpec as P


def stencil(padded, kap, speed_r, speed_p):
    n_r = padded.shape[1] - 4
    n_p = padded.shape[2] - 4

    def tap(a, b):
        return padded[:, 2 + a : 2 + a + n_r, 2 + b : 2 + b + n_p, :]

    centre = tap(0, 0)
    height = centre.shape[3]
    zpad = jnp.pad(centre, ((0, 0), (0, 0), (0, 0), (2, 2)))

    def ztap(a):
        return zpad[:, :, :, 2 + a : 2 + a + height]

    first_r = (tap(-2, 0) - 8.0 * tap(-1, 0) + 8.0 * tap(1, 0) - tap(2, 0)) / 12.0
    first_p = (tap(0, -2) - 8.0 * tap(0, -1) + 8.0 * tap(0, 1) - tap(0, 2)) / 12.0
    second_r = (
        -tap(-2, 0) + 16.0 * tap(-1, 0) - 30.0 * centre + 16.0 * tap(1, 0) - tap(2, 0)
    ) / 12.0
    second_p = (
        -tap(0, -2) + 16.0 * tap(0, -1) - 30.0 * centre + 16.0 * tap(0, 1) - tap(0, 2)
    ) / 12.0
    second_z = (-ztap(-2) + 16.0 * ztap(-1) - 30.0 * centre + 16.0 * ztap(1) - ztap(2)) / 12.0
    return (
        -speed_r[:, :, None, None] * first_r
        - speed_p[:, :, None, None] * first_p
        + kap[None] * (second_r + second_p + second_z)
    )


def split_stencil(cells, kap, speed_r, speed_p, width=2, core=False):
    sectors, rings = lax.axis_size("azi"), lax.axis_size("rad")
    rows, cols = cells.shape[-3], cells.shape[-2]
    left = lax.ppermute(cells[..., cols - width :, :], "azi", [(i, (i + 1) % sectors) for i in range(sectors)])
    right = lax.ppermute(cells[..., :width, :], "azi", [((i + 1) % sectors, i) for i in range(sectors)])
    above = lax.ppermute(cells[..., rows - width :, :, :], "rad", [(i, i + 1) for i in range(rings - 1)])
    below = lax.ppermute(cells[..., :width, :, :], "rad", [(i + 1, i) for i in range(rings - 1)])
    tall = jnp.concatenate([above, cells, below], axis=1)
    inner = kap[:, width : cols - width]
    if core:
        parts = [
            stencil(tall[:, : 3 * width], inner[:width], speed_r[:, :width], speed_p[:, :width]),
            stencil(cells, inner[width : rows - width], speed_r[:, width : rows - width], speed_p[:, width : rows - width]),
            stencil(tall[:, rows - width :], inner[rows - width :], speed_r[:, rows - width :], speed_p[:, rows - width :]),
        ]
        middle = jnp.concatenate(parts, axis=1)
    else:
        middle = stencil(tall, inner, speed_r, speed_p)
    edge = 2 * width

    def side(strip, near, far, pads):
        wide = jnp.concatenate([strip, near] if pads[0] else [near, strip], axis=2)
        corners = [(0, 0), (0, 0), pads, (0, 0)]
        tall = jnp.concatenate([jnp.pad(far[0], corners), wide, jnp.pad(far[1], corners)], axis=1)
        return tall

    low = side(left, cells[:, :, :edge], (above[:, :, :edge], below[:, :, :edge]), (width, 0))
    high = side(right, cells[:, :, cols - edge :], (above[:, :, cols - edge :], below[:, :, cols - edge :]), (0, width))
    first = stencil(low, kap[:, :width], speed_r, speed_p)
    last = stencil(high, kap[:, cols - width :], speed_r, speed_p)
    return jnp.concatenate([first, middle, last], axis=2)


def heun_sections(field, kappa, speed_r, speed_p, core=False):
    first = field + split_stencil(field, kappa, speed_r, speed_p, core=core)
    return 0.5 * (field + first + split_stencil(first, kappa, speed_r, speed_p))


def shift_rows(half, shifts):
    peers = lax.axis_size("azi")
    rows = half.shape[1]
    per = rows // peers
    full = lax.all_to_all(half, "azi", 1, 2, tiled=True)
    length = full.shape[2]
    first = lax.axis_index("azi") * per
    mine = lax.dynamic_slice_in_dim(shifts, first, per)
    doubled = jnp.concatenate([full, full], axis=2)
    rolled = []
    for row in range(per):
        start = (length - mine[row] % length) % length
        rolled.append(lax.dynamic_slice_in_dim(doubled[:, row], start, length, axis=1))
    moved = jnp.stack(rolled, axis=1)
    return lax.all_to_all(moved, "azi", 2, 1, tiled=True)


def shards(fields, kappa, radial_speed, azimuth_speed, shifts):
    half = heun_sections(fields, kappa, radial_speed, azimuth_speed, core=True)
    moved = shift_rows(half, shifts)
    return heun_sections(moved, kappa, radial_speed, azimuth_speed)


def solution(mesh):
    placed = (
        P(None, "rad", "azi", None),
        P("rad", "azi", None),
        P(None, "rad"),
        P(None, "rad"),
        P("rad"),
    )
    return jax.shard_map(
        shards, mesh=mesh, in_specs=placed, out_specs=P(None, "rad", "azi", None), check_vma=False
    )
```

```python
import jax
import jax.numpy as jnp
from jax import lax
from jax.sharding import PartitionSpec as P


def stencil(padded, kap, speed_r, speed_p):
    n_r = padded.shape[1] - 4
    n_p = padded.shape[2] - 4

    def tap(a, b):
        return padded[:, 2 + a : 2 + a + n_r, 2 + b : 2 + b + n_p, :]

    centre = tap(0, 0)
    height = centre.shape[3]
    zpad = jnp.pad(centre, ((0, 0), (0, 0), (0, 0), (2, 2)))

    def ztap(a):
        return zpad[:, :, :, 2 + a : 2 + a + height]

    first_r = (tap(-2, 0) - 8.0 * tap(-1, 0) + 8.0 * tap(1, 0) - tap(2, 0)) / 12.0
    first_p = (tap(0, -2) - 8.0 * tap(0, -1) + 8.0 * tap(0, 1) - tap(0, 2)) / 12.0
    second_r = (
        -tap(-2, 0) + 16.0 * tap(-1, 0) - 30.0 * centre + 16.0 * tap(1, 0) - tap(2, 0)
    ) / 12.0
    second_p = (
        -tap(0, -2) + 16.0 * tap(0, -1) - 30.0 * centre + 16.0 * tap(0, 1) - tap(0, 2)
    ) / 12.0
    second_z = (-ztap(-2) + 16.0 * ztap(-1) - 30.0 * centre + 16.0 * ztap(1) - ztap(2)) / 12.0
    return (
        -speed_r[:, :, None, None] * first_r
        - speed_p[:, :, None, None] * first_p
        + kap[None] * (second_r + second_p + second_z)
    )


def split_stencil(cells, kap, speed_r, speed_p, width=2):
    sectors, rings = lax.axis_size("azi"), lax.axis_size("rad")
    rows, cols = cells.shape[-3], cells.shape[-2]
    left = lax.ppermute(cells[..., cols - width :, :], "azi", [(i, (i + 1) % sectors) for i in range(sectors)])
    right = lax.ppermute(cells[..., :width, :], "azi", [((i + 1) % sectors, i) for i in range(sectors)])
    above = lax.ppermute(cells[..., rows - width :, :, :], "rad", [(i, i + 1) for i in range(rings - 1)])
    below = lax.ppermute(cells[..., :width, :, :], "rad", [(i + 1, i) for i in range(rings - 1)])
    tall = jnp.concatenate([above, cells, below], axis=1)
    inner = kap[:, width : cols - width]
    if rows > 4 * width:
        parts = [
            stencil(tall[:, : 3 * width], inner[:width], speed_r[:, :width], speed_p[:, :width]),
            stencil(cells, inner[width : rows - width], speed_r[:, width : rows - width], speed_p[:, width : rows - width]),
            stencil(tall[:, rows - width :], inner[rows - width :], speed_r[:, rows - width :], speed_p[:, rows - width :]),
        ]
        middle = jnp.concatenate(parts, axis=1)
    else:
        middle = stencil(tall, inner, speed_r, speed_p)
    edge = 2 * width

    def side(strip, near, far, pads):
        wide = jnp.concatenate([strip, near] if pads[0] else [near, strip], axis=2)
        corners = [(0, 0), (0, 0), pads, (0, 0)]
        tall = jnp.concatenate([jnp.pad(far[0], corners), wide, jnp.pad(far[1], corners)], axis=1)
        return tall

    low = side(left, cells[:, :, :edge], (above[:, :, :edge], below[:, :, :edge]), (width, 0))
    high = side(right, cells[:, :, cols - edge :], (above[:, :, cols - edge :], below[:, :, cols - edge :]), (0, width))
    first = stencil(low, kap[:, :width], speed_r, speed_p)
    last = stencil(high, kap[:, cols - width :], speed_r, speed_p)
    return jnp.concatenate([first, middle, last], axis=2)


def heun_sections(field, kappa, speed_r, speed_p):
    first = field + split_stencil(field, kappa, speed_r, speed_p)
    return 0.5 * (field + first + split_stencil(first, kappa, speed_r, speed_p))


def shift_rows(half, shifts):
    peers = lax.axis_size("azi")
    rows = half.shape[1]
    per = rows // peers
    full = lax.all_to_all(half, "azi", 1, 2, tiled=True)
    length = full.shape[2]
    first = lax.axis_index("azi") * per
    mine = lax.dynamic_slice_in_dim(shifts, first, per)
    doubled = jnp.concatenate([full, full], axis=2)
    rolled = []
    for row in range(per):
        start = (length - mine[row] % length) % length
        rolled.append(lax.dynamic_slice_in_dim(doubled[:, row], start, length, axis=1))
    moved = jnp.stack(rolled, axis=1)
    return lax.all_to_all(moved, "azi", 2, 1, tiled=True)


def shards(fields, kappa, radial_speed, azimuth_speed, shifts):
    half = heun_sections(fields, kappa, radial_speed, azimuth_speed)
    moved = shift_rows(half, shifts)
    return heun_sections(moved, kappa, radial_speed, azimuth_speed)


def solution(mesh):
    placed = (
        P(None, "rad", "azi", None),
        P("rad", "azi", None),
        P(None, "rad"),
        P(None, "rad"),
        P("rad"),
    )
    return jax.shard_map(
        shards, mesh=mesh, in_specs=placed, out_specs=P(None, "rad", "azi", None), check_vma=False
    )
```

```python
import jax
import jax.numpy as jnp
from jax import lax
from jax.sharding import PartitionSpec as P


def stencil(padded, kap, speed_r, speed_p):
    n_r = padded.shape[1] - 4
    n_p = padded.shape[2] - 4

    def tap(a, b):
        return padded[:, 2 + a : 2 + a + n_r, 2 + b : 2 + b + n_p, :]

    centre = tap(0, 0)
    height = centre.shape[3]
    zpad = jnp.pad(centre, ((0, 0), (0, 0), (0, 0), (2, 2)))

    def ztap(a):
        return zpad[:, :, :, 2 + a : 2 + a + height]

    first_r = (tap(-2, 0) - 8.0 * tap(-1, 0) + 8.0 * tap(1, 0) - tap(2, 0)) / 12.0
    first_p = (tap(0, -2) - 8.0 * tap(0, -1) + 8.0 * tap(0, 1) - tap(0, 2)) / 12.0
    second_r = (
        -tap(-2, 0) + 16.0 * tap(-1, 0) - 30.0 * centre + 16.0 * tap(1, 0) - tap(2, 0)
    ) / 12.0
    second_p = (
        -tap(0, -2) + 16.0 * tap(0, -1) - 30.0 * centre + 16.0 * tap(0, 1) - tap(0, 2)
    ) / 12.0
    second_z = (-ztap(-2) + 16.0 * ztap(-1) - 30.0 * centre + 16.0 * ztap(1) - ztap(2)) / 12.0
    return (
        -speed_r[:, :, None, None] * first_r
        - speed_p[:, :, None, None] * first_p
        + kap[None] * (second_r + second_p + second_z)
    )


def split_stencil(cells, kap, speed_r, speed_p, width=2, core=False, source=None):
    sectors, rings = lax.axis_size("azi"), lax.axis_size("rad")
    rows, cols = cells.shape[-3], cells.shape[-2]
    sent = cells if source is None else source
    left = lax.ppermute(sent[..., cols - width :, :], "azi", [(i, (i + 1) % sectors) for i in range(sectors)])
    right = lax.ppermute(sent[..., :width, :], "azi", [((i + 1) % sectors, i) for i in range(sectors)])
    above = lax.ppermute(sent[..., rows - width :, :, :], "rad", [(i, i + 1) for i in range(rings - 1)])
    below = lax.ppermute(sent[..., :width, :, :], "rad", [(i + 1, i) for i in range(rings - 1)])
    tall = jnp.concatenate([above, cells, below], axis=1)
    inner = kap[:, width : cols - width]
    if core:
        parts = [
            stencil(tall[:, : 3 * width], inner[:width], speed_r[:, :width], speed_p[:, :width]),
            stencil(cells, inner[width : rows - width], speed_r[:, width : rows - width], speed_p[:, width : rows - width]),
            stencil(tall[:, rows - width :], inner[rows - width :], speed_r[:, rows - width :], speed_p[:, rows - width :]),
        ]
        middle = jnp.concatenate(parts, axis=1)
    else:
        middle = stencil(tall, inner, speed_r, speed_p)
    edge = 2 * width

    def side(strip, near, far, pads):
        wide = jnp.concatenate([strip, near] if pads[0] else [near, strip], axis=2)
        corners = [(0, 0), (0, 0), pads, (0, 0)]
        tall = jnp.concatenate([jnp.pad(far[0], corners), wide, jnp.pad(far[1], corners)], axis=1)
        return tall

    low = side(left, cells[:, :, :edge], (above[:, :, :edge], below[:, :, :edge]), (width, 0))
    high = side(right, cells[:, :, cols - edge :], (above[:, :, cols - edge :], below[:, :, cols - edge :]), (0, width))
    first = stencil(low, kap[:, :width], speed_r, speed_p)
    last = stencil(high, kap[:, cols - width :], speed_r, speed_p)
    return jnp.concatenate([first, middle, last], axis=2)


def heun_sections(field, kappa, speed_r, speed_p, core=False):
    source = lax.optimization_barrier(field) if core else None
    first = field + split_stencil(field, kappa, speed_r, speed_p, core=core, source=source)
    return 0.5 * (field + first + split_stencil(first, kappa, speed_r, speed_p))


def shift_rows(half, shifts):
    peers = lax.axis_size("azi")
    rows = half.shape[1]
    per = rows // peers
    full = lax.all_to_all(half, "azi", 1, 2, tiled=True)
    length = full.shape[2]
    first = lax.axis_index("azi") * per
    mine = lax.dynamic_slice_in_dim(shifts, first, per)
    doubled = jnp.concatenate([full, full], axis=2)
    rolled = []
    for row in range(per):
        start = (length - mine[row] % length) % length
        rolled.append(lax.dynamic_slice_in_dim(doubled[:, row], start, length, axis=1))
    moved = jnp.stack(rolled, axis=1)
    return lax.all_to_all(moved, "azi", 2, 1, tiled=True)


def shards(fields, kappa, radial_speed, azimuth_speed, shifts):
    half = heun_sections(fields, kappa, radial_speed, azimuth_speed, core=True)
    moved = shift_rows(half, shifts)
    return heun_sections(moved, kappa, radial_speed, azimuth_speed)


def solution(mesh):
    placed = (
        P(None, "rad", "azi", None),
        P("rad", "azi", None),
        P(None, "rad"),
        P(None, "rad"),
        P("rad"),
    )
    return jax.shard_map(
        shards, mesh=mesh, in_specs=placed, out_specs=P(None, "rad", "azi", None), check_vma=False
    )
```

```python
import jax
import jax.numpy as jnp
from jax import lax
from jax.sharding import PartitionSpec as P


def stencil(padded, kap, speed_r, speed_p):
    n_r = padded.shape[1] - 4
    n_p = padded.shape[2] - 4

    def tap(a, b):
        return padded[:, 2 + a : 2 + a + n_r, 2 + b : 2 + b + n_p, :]

    centre = tap(0, 0)
    height = centre.shape[3]
    zpad = jnp.pad(centre, ((0, 0), (0, 0), (0, 0), (2, 2)))

    def ztap(a):
        return zpad[:, :, :, 2 + a : 2 + a + height]

    first_r = (tap(-2, 0) - 8.0 * tap(-1, 0) + 8.0 * tap(1, 0) - tap(2, 0)) / 12.0
    first_p = (tap(0, -2) - 8.0 * tap(0, -1) + 8.0 * tap(0, 1) - tap(0, 2)) / 12.0
    second_r = (
        -tap(-2, 0) + 16.0 * tap(-1, 0) - 30.0 * centre + 16.0 * tap(1, 0) - tap(2, 0)
    ) / 12.0
    second_p = (
        -tap(0, -2) + 16.0 * tap(0, -1) - 30.0 * centre + 16.0 * tap(0, 1) - tap(0, 2)
    ) / 12.0
    second_z = (-ztap(-2) + 16.0 * ztap(-1) - 30.0 * centre + 16.0 * ztap(1) - ztap(2)) / 12.0
    return (
        -speed_r[:, :, None, None] * first_r
        - speed_p[:, :, None, None] * first_p
        + kap[None] * (second_r + second_p + second_z)
    )


def split_stencil(cells, kap, speed_r, speed_p, width=2, core=False):
    sectors, rings = lax.axis_size("azi"), lax.axis_size("rad")
    rows, cols = cells.shape[-3], cells.shape[-2]
    left = lax.ppermute(cells[..., cols - width :, :], "azi", [(i, (i + 1) % sectors) for i in range(sectors)])
    right = lax.ppermute(cells[..., :width, :], "azi", [((i + 1) % sectors, i) for i in range(sectors)])
    above = lax.ppermute(cells[..., rows - width :, :, :], "rad", [(i, i + 1) for i in range(rings - 1)])
    below = lax.ppermute(cells[..., :width, :, :], "rad", [(i + 1, i) for i in range(rings - 1)])
    tall = jnp.concatenate([above, cells, below], axis=1)
    inner = kap[:, width : cols - width]
    if core:
        parts = [
            stencil(tall[:, : 3 * width], inner[:width], speed_r[:, :width], speed_p[:, :width]),
            stencil(cells, inner[width : rows - width], speed_r[:, width : rows - width], speed_p[:, width : rows - width]),
            stencil(tall[:, rows - width :], inner[rows - width :], speed_r[:, rows - width :], speed_p[:, rows - width :]),
        ]
        middle = jnp.concatenate(parts, axis=1)
    else:
        middle = stencil(tall, inner, speed_r, speed_p)
    edge = 2 * width

    def side(strip, near, far, pads):
        wide = jnp.concatenate([strip, near] if pads[0] else [near, strip], axis=2)
        corners = [(0, 0), (0, 0), pads, (0, 0)]
        tall = jnp.concatenate([jnp.pad(far[0], corners), wide, jnp.pad(far[1], corners)], axis=1)
        return tall

    low = side(left, cells[:, :, :edge], (above[:, :, :edge], below[:, :, :edge]), (width, 0))
    high = side(right, cells[:, :, cols - edge :], (above[:, :, cols - edge :], below[:, :, cols - edge :]), (0, width))
    first = stencil(low, kap[:, :width], speed_r, speed_p)
    last = stencil(high, kap[:, cols - width :], speed_r, speed_p)
    start = jnp.minimum(lax.axis_index("rad"), 0) + width
    return jnp.concatenate([first, middle, last], axis=2), lax.dynamic_slice_in_dim(tall, start, rows, axis=1)


def heun_sections(field, kappa, speed_r, speed_p, core=False):
    change, held = split_stencil(field, kappa, speed_r, speed_p, core=core)
    first = held + change
    return 0.5 * (held + first + split_stencil(first, kappa, speed_r, speed_p)[0])


def shift_rows(half, shifts):
    peers = lax.axis_size("azi")
    rows = half.shape[1]
    per = rows // peers
    full = lax.all_to_all(half, "azi", 1, 2, tiled=True)
    length = full.shape[2]
    first = lax.axis_index("azi") * per
    mine = lax.dynamic_slice_in_dim(shifts, first, per)
    doubled = jnp.concatenate([full, full], axis=2)
    rolled = []
    for row in range(per):
        start = (length - mine[row] % length) % length
        rolled.append(lax.dynamic_slice_in_dim(doubled[:, row], start, length, axis=1))
    moved = jnp.stack(rolled, axis=1)
    return lax.all_to_all(moved, "azi", 2, 1, tiled=True)


def shards(fields, kappa, radial_speed, azimuth_speed, shifts):
    half = heun_sections(fields, kappa, radial_speed, azimuth_speed, core=True)
    moved = shift_rows(half, shifts)
    return heun_sections(moved, kappa, radial_speed, azimuth_speed)


def solution(mesh):
    placed = (
        P(None, "rad", "azi", None),
        P("rad", "azi", None),
        P(None, "rad"),
        P(None, "rad"),
        P("rad"),
    )
    return jax.shard_map(
        shards, mesh=mesh, in_specs=placed, out_specs=P(None, "rad", "azi", None), check_vma=False
    )
```
